512 devices in a mesh: seq: 8 (over x, core), tp: 16 (over z), req: 4 (over y).
Axes of the slice: x: 4, y: 4, z: 16, core: 2. Of those that a mesh axis runs over, the one named last changes fastest.
Arguments:
- tokens: bfloat16 [32768, 1792], P(('req', 'seq'), 'tp'), parts along dimension 0, may hold values from -6 to 6
- w_in: bfloat16 [1792, 4096], P(None, 'tp'), may hold values from -0.125 to 0.125
- conv_w: float32 [3, 1792], P(None, 'tp'), may hold values from -3 to 3
- head_gain: float32 [1792], P('tp'), may hold values from 0.1 to 1.9
- w_out: bfloat16 [1792, 1792], P('tp'), may hold values from -0.125 to 0.125
- prompt_lens: int32 [16], P('req'), parts along dimension 0, may hold values from 1 to 4096, 8192 in all
- req_group: int32 [128], P('req'), parts along dimension 0, may hold values from 0 to 3, as said below
- row_request: int32 [128], P('req'), parts along dimension 0, may hold values from 0 to 31, each once
Outputs:
- mixed: bfloat16 [32768, 1792], P(('req', 'seq'), 'tp'), parts along dimension 0
- req_state: float32 [128, 16, 273, 112], P(('req', 'seq'), 'tp'), parts along dimension 0
- req_norm: float32 [128, 16, 273], P(('req', 'seq'), 'tp'), parts along dimension 0
- req_edge: bfloat16 [128, 2, 1792], P(('req', 'seq'), None, 'tp'), parts along dimension 0
The draws below stay inside these ranges and needn't reach their ends.
There are 4 independent parts, one for each index of `req`. The reference program is written for one: setup_inputs(seed, part) draws one part's arguments, and reference() takes and returns one part's arrays. A program takes and returns all parts, laid end to end along the dimension named above; an argument that names none is the same for every part. Nothing has to cross between parts.
Inputs may be any that keep to these rules, and one draw needn't show every extreme that they name: `prompt_lens`: the lengths sum to 8192, and the largest is half of 8192. `req_group`: every one of the 4 prompts is shared by at least one request. `row_request`: each request appears once; rows i * 4 to (i + 1) * 4 - 1 lie on index i of seq.
All inputs are finite; a program needn't handle non-finite values.
Results may differ from the reference program's by a relative error of at most 0.019.
Values may be sent and summed in bfloat16 or wider, within the bound.
No kernel may reach another device: no remote copies, remote signals or barrier semaphores. Data moves between devices by JAX's collectives and lax.ppermute only.
A program may use at most 64 MiB of HBM per device.

```python
import math
import jax
import jax.numpy as jnp
import numpy as np
from jax import lax

D = 1792
H = 16
FEAT = 16
HD = 112
FMAP = 273
KW = 3
PROMPTS = 4
TOK_DEV = 1024
TOKENS = 8192
REQS = 32
N_TP = 16


def draw_req_group(key, part):
    named = jnp.arange(PROMPTS, dtype=jnp.int32)
    extra = jax.random.randint(jax.random.fold_in(key, 11), (REQS - PROMPTS,), 0, PROMPTS, dtype=jnp.int32)
    return jax.random.permutation(jax.random.fold_in(key, 12), jnp.concatenate([named, extra], 0))


def block_scale(rng, dims, shards, least, largest):
    factor_of = 1.0
    for position, shards_of in shards:
        steps = jax.random.uniform(jax.random.fold_in(jax.random.fold_in(rng, 6), position), (shards_of,), jnp.float32, least / len(shards), largest / len(shards))
        factor_of = factor_of * jnp.repeat(jnp.exp(steps), dims[position] // shards_of).reshape((-1,) + (1,) * (len(dims) - 1 - position))
    return factor_of


def split_up(number_of, total, limit, lean):
    loads = [(1 << 20) // math.isqrt(rank ** lean) + 1 for rank in range(2, number_of + 1)]
    surplus, counts = total - limit - (number_of - 1), [1] * (number_of - 1)
    while surplus > 0:
        free = [i for i in range(number_of - 1) if counts[i] < limit]
        whole, left = sum([loads[i] for i in free]), surplus
        for i in free:
            more = min(limit - counts[i], max(1, left * loads[i] // whole), surplus)
            counts[i] = counts[i] + more
            surplus = surplus - more
    return np.array([limit] + counts)


def uneven_parts(key, number_of, total, limit, lean):
    if number_of == 2:
        one = jax.random.randint(key, (), max(1, total - limit), min(limit, total - 1) + 1)
        return jnp.stack([one, total - one])
    tallies = jnp.asarray(split_up(number_of, total, limit, lean), jnp.int32)
    twos = (number_of - 1) // 2
    donor, taker = tallies[1:1 + 2 * twos:2], tallies[2:2 + 2 * twos:2]
    slack = jnp.minimum(donor - 1, limit - taker)
    shifted = jax.random.randint(jax.random.fold_in(key, 1), (twos,), 0, 1 << 20) % (slack + 1)
    tallies = tallies.at[1:1 + 2 * twos:2].set(donor - shifted).at[2:2 + 2 * twos:2].set(taker + shifted)
    return tallies[jax.random.permutation(jax.random.fold_in(key, 2), number_of)]


def centred(stream_key, extent, deviation, most, pieces=(), kind=jnp.bfloat16):
    array = jax.random.normal(stream_key, extent, jnp.float32) * deviation
    if len(pieces) > 0:
        array = block_scale(stream_key, extent, pieces, -0.22, 0.18) * array
    return jnp.clip(array, min=-most, max=most).astype(kind)


def setup_inputs(seed: int = 0, part: int = 0) -> dict:
    seeds = jax.random.split(jax.random.key(seed), 9)
    own_keys = jax.random.split(jax.random.fold_in(seeds[8], part), 9)
    tokens = centred(own_keys[0], (TOKENS, D), 1.0, 6.0, ((0, 8), (1, 16)))
    w_in = centred(seeds[1], (D, H * (2 * FEAT + 2 * HD)), D ** -0.5, 0.125, ((1, 16),))
    conv_w = centred(seeds[2], (KW, H * HD), 0.6, 3.0, ((1, 16),), jnp.float32)
    head_gain = jnp.clip(1.0 + 0.18 * jax.random.normal(seeds[3], (H * HD,), jnp.float32), 0.1, 1.9)
    w_out = centred(seeds[4], (H * HD, D), (H * HD) ** -0.5, 0.125, ((0, 16),))
    prompt_lens = uneven_parts(own_keys[5], PROMPTS, TOKENS, TOKENS // 2, 2).astype(jnp.int32)
    req_group = draw_req_group(jax.random.fold_in(jax.random.fold_in(seeds[8], part), 71), part)
    row_request = jax.random.permutation(own_keys[7], REQS).astype(jnp.int32)
    return dict(tokens=tokens, w_in=w_in, conv_w=conv_w, head_gain=head_gain, w_out=w_out, prompt_lens=prompt_lens, req_group=req_group, row_request=row_request)


EPS = 1e-05
HIGH = lax.Precision.HIGHEST

def taylor_map(values):
    size = values.shape[-1]
    ones = jnp.ones(values.shape[:-1] + (1,), jnp.float32)
    pairs = (values[..., :, None] * values[..., None, :]).reshape(values.shape[:-1] + (size * size,))
    return jnp.concatenate([ones, values, pairs * 0.5 ** 0.5], axis=-1)

def segment_ids(positions, ends):
    return lax.optimization_barrier(jnp.sum((positions[:, None] >= ends[None, :]).astype(jnp.int32), axis=1))

def reference(tokens, w_in, conv_w, head_gain, w_out, prompt_lens, req_group, row_request):
    width = 2 * FEAT + 2 * HD
    total_rows = tokens.shape[0]
    blocks = total_rows // TOK_DEV
    proj = jnp.dot(tokens, w_in, preferred_element_type=jnp.float32).astype(jnp.bfloat16)
    proj = proj.reshape(total_rows, H, width)
    ends = jnp.cumsum(prompt_lens).astype(jnp.int32)
    starts = (ends - prompt_lens).astype(jnp.int32)
    positions = jnp.arange(total_rows, dtype=jnp.int32)
    seg = segment_ids(positions, ends)
    gate_pre = proj[:, :, 2 * FEAT + HD:].reshape(total_rows, H * HD)
    padded = jnp.concatenate([jnp.zeros((KW - 1, H * HD), jnp.bfloat16), gate_pre], 0)
    seg_pad = jnp.concatenate([jnp.full((KW - 1,), -1, jnp.int32), seg], 0)
    gate = jnp.zeros((total_rows, H * HD), jnp.float32)
    for tap in range(KW):
        low = KW - 1 - tap
        same = (seg_pad[low:low + total_rows] == seg).astype(jnp.float32)
        gate = gate + conv_w[tap][None, :] * padded[low:low + total_rows].astype(jnp.float32) * same[:, None]
    group_rows = H // N_TP * HD
    out_groups = w_out.reshape(N_TP, group_rows, D).astype(jnp.float32)
    gain = head_gain.reshape(H, HD)

    def block_step(carry, inputs):
        state, group_state, group_norm = carry
        proj_b, gate_b, seg_b, index = inputs
        first_row = index * TOK_DEV
        pos_b = first_row + jnp.arange(TOK_DEV, dtype=jnp.int32)
        qs = proj_b[:, :, :FEAT].astype(jnp.float32) * FEAT ** (-0.25)
        ks = proj_b[:, :, FEAT:2 * FEAT].astype(jnp.float32) * FEAT ** (-0.25)
        values = proj_b[:, :, 2 * FEAT:2 * FEAT + HD].astype(jnp.float32)
        dots = jnp.einsum('thf,shf->hts', qs, ks, precision=HIGH)
        visible = ((pos_b[None, :] <= pos_b[:, None]) & (seg_b[:, None] == seg_b[None, :])).astype(jnp.float32)
        weights = (1.0 + dots + 0.5 * dots * dots) * visible[None]
        rounded = lax.optimization_barrier(weights.astype(jnp.bfloat16)).astype(jnp.float32)
        numer = jnp.einsum('hts,shd->thd', rounded, values, precision=HIGH)
        phi_q = taylor_map(qs)
        phi_k = taylor_map(ks)
        seg_before = jnp.sum((first_row - 1 >= ends).astype(jnp.int32))
        carried = ((seg_b == seg_before) & (first_row > 0)).astype(jnp.float32)
        attended = numer + jnp.einsum('thf,hfd->thd', phi_q, state, precision=HIGH) * carried[:, None, None]
        inv_rms = lax.rsqrt(lax.optimization_barrier(jnp.mean(attended * attended, axis=2, keepdims=True)) + EPS)
        gate_b3 = gate_b.reshape(TOK_DEV, H, HD)
        hidden = (attended * inv_rms * gain[None] * jax.nn.silu(gate_b3)).astype(jnp.bfloat16)
        partial_value = jnp.einsum('tgc,gcd->gtd', hidden.reshape(TOK_DEV, N_TP, group_rows).astype(jnp.float32), out_groups, precision=HIGH)
        partial_value = lax.optimization_barrier(partial_value.astype(jnp.bfloat16)).astype(jnp.float32)
        mixed_b = lax.optimization_barrier(jnp.sum(partial_value, axis=0)).astype(jnp.bfloat16)
        tail = (seg_b == seg_b[-1]).astype(jnp.float32)
        tail_keys = phi_k * tail[:, None, None]
        tail_state = jnp.einsum('thf,thd->hfd', tail_keys, values, precision=HIGH)
        restart = jnp.any((starts >= first_row) & (starts < first_row + TOK_DEV)).astype(jnp.float32)
        state = tail_state + (1.0 - restart) * state
        onehot = (seg_b[:, None] == jnp.arange(PROMPTS, dtype=jnp.int32)[None, :]).astype(jnp.float32)
        group_state = group_state + jnp.einsum('tg,thf,thd->ghfd', onehot, phi_k, values, precision=HIGH)
        group_norm = group_norm + jnp.einsum('tg,thf->ghf', onehot, phi_k, precision=HIGH)
        return ((state, group_state, group_norm), mixed_b)
    init = (jnp.zeros((H, FMAP, HD), jnp.float32), jnp.zeros((PROMPTS, H, FMAP, HD), jnp.float32), jnp.zeros((PROMPTS, H, FMAP), jnp.float32))
    inputs = (proj.reshape(blocks, TOK_DEV, H, width), gate.reshape(blocks, TOK_DEV, H * HD), seg.reshape(blocks, TOK_DEV), jnp.arange(blocks, dtype=jnp.int32))
    final, mixed_blocks = lax.scan(block_step, init, inputs)
    group_state, group_norm = (final[1], final[2])
    mixed = mixed_blocks.reshape(total_rows, D)
    offsets = jnp.arange(KW - 1, dtype=jnp.int32)
    rows = ends[:, None] - (KW - 1) + offsets[None, :]
    valid = rows >= starts[:, None]
    edge = jnp.where(valid[:, :, None], gate_pre[jnp.clip(rows, 0, total_rows - 1)], jnp.zeros((), jnp.bfloat16))
    groups = req_group[row_request]
    scale = lax.rsqrt(prompt_lens.astype(jnp.float32))
    req_state = group_state[groups] * scale[groups][:, None, None, None]
    req_norm = group_norm[groups] * scale[groups][:, None, None]
    req_edge = edge[groups].astype(jnp.bfloat16)
    return (mixed, req_state, req_norm, req_edge)
```

```python
import jax
import jax.numpy as jnp
from jax import lax
from jax.sharding import PartitionSpec as P

FEAT = 16
HD = 112
KW = 3
PROMPTS = 4
SLOTS = 4


EPS = 1e-05
HIGH = lax.Precision.HIGHEST


def passed_along(shard, axis, by):
    size = lax.axis_size(axis)
    pairs = [(i, i + by) for i in range(size) if 0 <= i + by < size]
    return lax.ppermute(shard, axis, pairs)


def scan_blocks(parts, axis):
    size, here = (lax.axis_size(axis), lax.axis_index(axis))
    total = [p.astype(jnp.float32) for p in parts]
    before = [jnp.zeros_like(t) for t in total]
    step = 1
    while step < size:
        pairs = [(i, i ^ step) for i in range(size)]
        got = lax.ppermute(tuple(t.astype(jnp.bfloat16) for t in total), axis, pairs)
        got = [g.astype(jnp.float32) for g in got]
        lower = ((here ^ step) < here).astype(jnp.float32)
        before = [b + lower * g for b, g in zip(before, got)]
        total = [t + g for t, g in zip(total, got)]
        step *= 2
    return before, total


def taylor_map(values):
    size = values.shape[-1]
    ones = jnp.ones(values.shape[:-1] + (1,), jnp.float32)
    pairs = (values[..., :, None] * values[..., None, :]).reshape(
        values.shape[:-1] + (size * size,)
    )
    return jnp.concatenate([ones, values, pairs * 0.5**0.5], axis=-1)


def segment_ids(positions, ends):
    return jnp.sum((positions[:, None] >= ends[None, :]).astype(jnp.int32), axis=1)


def local(tokens, w_in, conv_w, head_gain, w_out, prompt_lens, req_group, row_request):
    tok_rows = tokens.shape[0]
    width = 2 * FEAT + 2 * HD
    local_heads = w_in.shape[1] // width
    local_cols = local_heads * HD
    seq_pos = lax.axis_index("seq")
    first_row = seq_pos * tok_rows
    ends = jnp.cumsum(prompt_lens)
    starts = ends - prompt_lens
    positions = first_row + jnp.arange(tok_rows, dtype=jnp.int32)
    seg = segment_ids(positions, ends)
    proj = jnp.dot(
        lax.all_gather(tokens, "tp", axis=1, tiled=True), w_in, preferred_element_type=jnp.float32
    )
    proj = proj.astype(jnp.bfloat16).reshape(tok_rows, local_heads, width)
    gate_pre = proj[:, :, 2 * FEAT + HD :].reshape(tok_rows, local_cols)
    rim = passed_along(gate_pre[tok_rows - (KW - 1) :], "seq", 1)
    extended = jnp.concatenate([rim, gate_pre], 0)
    ext_pos = first_row - (KW - 1) + jnp.arange(tok_rows + KW - 1, dtype=jnp.int32)
    ext_seg = segment_ids(ext_pos, ends)
    gate = jnp.zeros((tok_rows, local_cols), jnp.float32)
    for tap in range(KW):
        low = KW - 1 - tap
        same = (ext_seg[low : low + tok_rows] == seg).astype(jnp.float32)
        gate = (
            gate
            + conv_w[tap][None, :]
            * extended[low : low + tok_rows].astype(jnp.float32)
            * same[:, None]
        )
    qs_b = proj[:, :, :FEAT] * jnp.bfloat16(FEAT ** (-0.25))
    ks_b = proj[:, :, FEAT : 2 * FEAT] * jnp.bfloat16(FEAT ** (-0.25))
    qs = qs_b.astype(jnp.float32)
    ks = ks_b.astype(jnp.float32)
    values = proj[:, :, 2 * FEAT : 2 * FEAT + HD]
    values_f = values.astype(jnp.float32)
    dots = jnp.einsum("thf,shf->hts", qs_b, ks_b, preferred_element_type=jnp.float32)
    visible = (positions[None, :] <= positions[:, None]) & (seg[:, None] == seg[None, :])
    weights = jnp.where(visible[None], 1.0 + dots + 0.5 * dots * dots, 0.0)
    numer = jnp.einsum(
        "hts,shd->thd", weights.astype(jnp.bfloat16), values, preferred_element_type=jnp.float32
    )
    phi_q = taylor_map(qs)
    phi_k = taylor_map(ks)
    fmap = phi_k.shape[-1]
    prompt_index = jnp.arange(PROMPTS, dtype=jnp.int32)
    onehot = (seg[:, None] == prompt_index[None, :]).astype(jnp.float32)
    keyed = (onehot[:, :, None, None] * phi_k[:, None, :, :]).reshape(
        tok_rows, PROMPTS * local_heads * fmap
    )
    contrib_state = lax.dot_general(
        keyed.reshape(tok_rows, PROMPTS, local_heads, fmap),
        values_f,
        (((0,), (0,)), ((2,), (1,))),
        precision=HIGH,
    )
    contrib_norm = jnp.einsum("tg,thf->ghf", onehot, phi_k, precision=HIGH)
    offsets = jnp.arange(KW - 1, dtype=jnp.int32)
    edge_rows = ends[:, None] - (KW - 1) + offsets[None, :]
    edge_valid = edge_rows >= starts[:, None]
    match = ((positions[:, None, None] == edge_rows[None]) & edge_valid[None]).astype(jnp.bfloat16)
    contrib_edge = jnp.einsum("tgj,tc->gjc", match, gate_pre, preferred_element_type=jnp.float32)
    (pre_state, _, _), (all_state, all_norm, all_edge) = scan_blocks(
        (contrib_state, contrib_norm, contrib_edge), "seq"
    )
    seg_before = jnp.sum((first_row - 1 >= ends).astype(jnp.int32))
    carry_state = lax.dynamic_index_in_dim(pre_state, seg_before, axis=1, keepdims=False)
    carried = ((seg == seg_before) & (first_row > 0)).astype(jnp.float32)
    attended = (
        numer
        + jnp.einsum("thf,hfd->thd", phi_q, carry_state, precision=HIGH) * carried[:, None, None]
    )
    inv_rms = lax.rsqrt(jnp.mean(attended * attended, axis=2, keepdims=True) + EPS)
    gain = head_gain.reshape(local_heads, HD)
    hidden = (
        attended * inv_rms * gain[None] * jax.nn.silu(gate.reshape(tok_rows, local_heads, HD))
    ).astype(jnp.bfloat16)
    hidden = hidden.reshape(tok_rows, local_cols)
    product = lax.dot_general(
        w_out, hidden, (((0,), (1,)), ((), ())), preferred_element_type=jnp.float32
    )
    summed = lax.psum_scatter(
        lax.optimization_barrier(product.astype(jnp.bfloat16))
        .astype(jnp.float32)
        .astype(jnp.bfloat16),
        "tp",
        scatter_dimension=0,
        tiled=True,
    ).astype(jnp.float32)
    mixed = summed.T.astype(jnp.bfloat16)
    scale = lax.rsqrt(prompt_lens.astype(jnp.float32))
    my_requests = lax.dynamic_slice_in_dim(row_request, seq_pos * SLOTS, SLOTS)
    my_groups = jnp.take(req_group, my_requests)
    my_scale = jnp.take(scale, my_groups)
    req_state = jnp.take(all_state, my_groups, axis=1).transpose(1, 0, 2, 3) * my_scale[
        :, None, None, None
    ]
    req_norm = jnp.take(all_norm, my_groups, axis=0) * my_scale[:, None, None]
    req_edge = jnp.take(all_edge, my_groups, axis=0).astype(jnp.bfloat16)
    return (mixed, req_state, req_norm, req_edge)


def solution(mesh):
    in_specs = (
        P(("req", "seq"), "tp"),
        P(None, "tp"),
        P(None, "tp"),
        P("tp"),
        P("tp", None),
        P("req"),
        P("req"),
        P("req"),
    )
    out_specs = (
        P(("req", "seq"), "tp"),
        P(("req", "seq"), "tp", None, None),
        P(("req", "seq"), "tp", None),
        P(("req", "seq"), None, "tp"),
    )
    return jax.shard_map(local, mesh=mesh, in_specs=in_specs, out_specs=out_specs, check_vma=False)
```

```python
import jax
import jax.numpy as jnp
from jax import lax
from jax.sharding import PartitionSpec as P

FEAT = 16
HD = 112
KW = 3
PROMPTS = 4
SLOTS = 4


EPS = 1e-05
HIGH = lax.Precision.HIGHEST


def passed_along(shard, axis, by):
    size = lax.axis_size(axis)
    pairs = [(i, i + by) for i in range(size) if 0 <= i + by < size]
    return lax.ppermute(shard, axis, pairs)


def psum_doubling(parts, axis):
    size = lax.axis_size(axis)
    total = [p.astype(jnp.float32) for p in parts]
    step = 1
    while step < size:
        pairs = [(i, i ^ step) for i in range(size)]
        got = lax.ppermute(tuple(t.astype(jnp.bfloat16) for t in total), axis, pairs)
        total = [t + g.astype(jnp.float32) for t, g in zip(total, got)]
        step *= 2
    return total


def tail_prefix(tail, tail_seg, axis):
    size, here = (lax.axis_size(axis), lax.axis_index(axis))
    seg_before = tail_seg[jnp.maximum(here - 1, 0)]
    group = tail.astype(jnp.float32)
    before = jnp.zeros_like(group)
    step = 1
    while step < size:
        pairs = [(i, i ^ step) for i in range(size)]
        got = lax.ppermute(group.astype(jnp.bfloat16), axis, pairs).astype(jnp.float32)
        other = here ^ step
        my_end = (here | (step - 1))
        other_end = (other | (step - 1))
        same = (tail_seg[my_end] == tail_seg[other_end]).astype(jnp.float32)
        earlier = other < here
        take = (earlier & (tail_seg[other_end] == seg_before)).astype(jnp.float32)
        before = before + take * got
        group = jnp.where(earlier, group + same * got, got + same * group)
        step *= 2
    return before


def taylor_map(values):
    size = values.shape[-1]
    ones = jnp.ones(values.shape[:-1] + (1,), jnp.float32)
    pairs = (values[..., :, None] * values[..., None, :]).reshape(
        values.shape[:-1] + (size * size,)
    )
    return jnp.concatenate([ones, values, pairs * 0.5**0.5], axis=-1)


def segment_ids(positions, ends):
    return jnp.sum((positions[:, None] >= ends[None, :]).astype(jnp.int32), axis=1)


def local(tokens, w_in, conv_w, head_gain, w_out, prompt_lens, req_group, row_request):
    tok_rows = tokens.shape[0]
    width = 2 * FEAT + 2 * HD
    local_heads = w_in.shape[1] // width
    local_cols = local_heads * HD
    seq_pos = lax.axis_index("seq")
    first_row = seq_pos * tok_rows
    ends = jnp.cumsum(prompt_lens)
    starts = ends - prompt_lens
    positions = first_row + jnp.arange(tok_rows, dtype=jnp.int32)
    seg = segment_ids(positions, ends)
    proj = jnp.dot(
        lax.all_gather(tokens, "tp", axis=1, tiled=True), w_in, preferred_element_type=jnp.float32
    )
    proj = proj.astype(jnp.bfloat16).reshape(tok_rows, local_heads, width)
    gate_pre = proj[:, :, 2 * FEAT + HD :].reshape(tok_rows, local_cols)
    rim = passed_along(gate_pre[tok_rows - (KW - 1) :], "seq", 1)
    extended = jnp.concatenate([rim, gate_pre], 0)
    ext_pos = first_row - (KW - 1) + jnp.arange(tok_rows + KW - 1, dtype=jnp.int32)
    ext_seg = segment_ids(ext_pos, ends)
    gate = jnp.zeros((tok_rows, local_cols), jnp.float32)
    for tap in range(KW):
        low = KW - 1 - tap
        same = (ext_seg[low : low + tok_rows] == seg).astype(jnp.float32)
        gate = (
            gate
            + conv_w[tap][None, :]
            * extended[low : low + tok_rows].astype(jnp.float32)
            * same[:, None]
        )
    qs_b = proj[:, :, :FEAT] * jnp.bfloat16(FEAT ** (-0.25))
    ks_b = proj[:, :, FEAT : 2 * FEAT] * jnp.bfloat16(FEAT ** (-0.25))
    qs = qs_b.astype(jnp.float32)
    ks = ks_b.astype(jnp.float32)
    values = proj[:, :, 2 * FEAT : 2 * FEAT + HD]
    values_f = values.astype(jnp.float32)
    dots = jnp.einsum("thf,shf->hts", qs_b, ks_b, preferred_element_type=jnp.float32)
    visible = (positions[None, :] <= positions[:, None]) & (seg[:, None] == seg[None, :])
    weights = jnp.where(visible[None], 1.0 + dots + 0.5 * dots * dots, 0.0)
    numer = jnp.einsum(
        "hts,shd->thd", weights.astype(jnp.bfloat16), values, preferred_element_type=jnp.float32
    )
    phi_q = taylor_map(qs)
    phi_k = taylor_map(ks)
    fmap = phi_k.shape[-1]
    prompt_index = jnp.arange(PROMPTS, dtype=jnp.int32)
    onehot = (seg[:, None] == prompt_index[None, :]).astype(jnp.float32)
    keyed = (onehot[:, :, None, None] * phi_k[:, None, :, :]).reshape(
        tok_rows, PROMPTS * local_heads * fmap
    )
    contrib_state = lax.dot_general(
        keyed.reshape(tok_rows, PROMPTS, local_heads, fmap),
        values_f,
        (((0,), (0,)), ((2,), (1,))),
        precision=HIGH,
    )
    contrib_norm = jnp.einsum("tg,thf->ghf", onehot, phi_k, precision=HIGH)
    offsets = jnp.arange(KW - 1, dtype=jnp.int32)
    edge_rows = ends[:, None] - (KW - 1) + offsets[None, :]
    edge_valid = edge_rows >= starts[:, None]
    match = ((positions[:, None, None] == edge_rows[None]) & edge_valid[None]).astype(jnp.bfloat16)
    contrib_edge = jnp.einsum("tgj,tc->gjc", match, gate_pre, preferred_element_type=jnp.float32)
    block_ends = (jnp.arange(lax.axis_size("seq"), dtype=jnp.int32) + 1) * tok_rows - 1
    tail_seg = segment_ids(block_ends, ends)
    seg_last = tail_seg[seq_pos]
    tail_state = lax.dynamic_index_in_dim(contrib_state, seg_last, axis=1, keepdims=False)
    carry_state = tail_prefix(tail_state, tail_seg, "seq")
    seg_before = jnp.sum((first_row - 1 >= ends).astype(jnp.int32))
    carried = ((seg == seg_before) & (first_row > 0)).astype(jnp.float32)
    attended = (
        numer
        + jnp.einsum("thf,hfd->thd", phi_q, carry_state, precision=HIGH) * carried[:, None, None]
    )
    inv_rms = lax.rsqrt(jnp.mean(attended * attended, axis=2, keepdims=True) + EPS)
    gain = head_gain.reshape(local_heads, HD)
    hidden = (
        attended * inv_rms * gain[None] * jax.nn.silu(gate.reshape(tok_rows, local_heads, HD))
    ).astype(jnp.bfloat16)
    hidden = hidden.reshape(tok_rows, local_cols)
    product = jnp.einsum(
        "tk,kgc->gtc",
        hidden,
        w_out.reshape(local_cols, lax.axis_size("tp"), -1),
        preferred_element_type=jnp.float32,
    )
    summed = lax.psum_scatter(
        lax.optimization_barrier(product.astype(jnp.bfloat16))
        .astype(jnp.float32)
        .astype(jnp.bfloat16),
        "tp",
        scatter_dimension=0,
        tiled=True,
    )
    mixed = summed.reshape(tok_rows, -1)
    all_state, all_norm, all_edge = psum_doubling((contrib_state, contrib_norm, contrib_edge), "seq")
    scale = lax.rsqrt(prompt_lens.astype(jnp.float32))
    my_requests = lax.dynamic_slice_in_dim(row_request, seq_pos * SLOTS, SLOTS)
    my_groups = jnp.take(req_group, my_requests)
    my_scale = jnp.take(scale, my_groups)
    req_state = jnp.take(all_state, my_groups, axis=1).transpose(1, 0, 2, 3) * my_scale[
        :, None, None, None
    ]
    req_norm = jnp.take(all_norm, my_groups, axis=0) * my_scale[:, None, None]
    req_edge = jnp.take(all_edge, my_groups, axis=0).astype(jnp.bfloat16)
    return (mixed, req_state, req_norm, req_edge)


def solution(mesh):
    in_specs = (
        P(("req", "seq"), "tp"),
        P(None, "tp"),
        P(None, "tp"),
        P("tp"),
        P("tp", None),
        P("req"),
        P("req"),
        P("req"),
    )
    out_specs = (
        P(("req", "seq"), "tp"),
        P(("req", "seq"), "tp", None, None),
        P(("req", "seq"), "tp", None),
        P(("req", "seq"), None, "tp"),
    )
    return jax.shard_map(local, mesh=mesh, in_specs=in_specs, out_specs=out_specs, check_vma=False)
```

```python
import jax
import jax.numpy as jnp
from jax import lax
from jax.sharding import PartitionSpec as P

FEAT = 16
HD = 112
KW = 3
PROMPTS = 4
SLOTS = 4


EPS = 1e-05
HIGH = lax.Precision.HIGHEST


def passed_along(shard, axis, by):
    size = lax.axis_size(axis)
    pairs = [(i, i + by) for i in range(size) if 0 <= i + by < size]
    return lax.ppermute(shard, axis, pairs)


def psum_doubling(parts, axis):
    size = lax.axis_size(axis)
    total = [p.astype(jnp.float32) for p in parts]
    step = 1
    while step < size:
        pairs = [(i, i ^ step) for i in range(size)]
        got = lax.ppermute(tuple(t.astype(jnp.bfloat16) for t in total), axis, pairs)
        total = [t + g.astype(jnp.float32) for t, g in zip(total, got)]
        step *= 2
    return total


def tail_prefix(tail, tail_seg, axis):
    size, here = (lax.axis_size(axis), lax.axis_index(axis))
    seg_before = tail_seg[jnp.maximum(here - 1, 0)]
    group = tail.astype(jnp.float32)
    before = jnp.zeros_like(group)
    step = 1
    while step < size:
        pairs = [(i, i ^ step) for i in range(size)]
        got = lax.ppermute(group.astype(jnp.bfloat16), axis, pairs).astype(jnp.float32)
        other = here ^ step
        my_end = (here | (step - 1))
        other_end = (other | (step - 1))
        same = (tail_seg[my_end] == tail_seg[other_end]).astype(jnp.float32)
        earlier = other < here
        take = (earlier & (tail_seg[other_end] == seg_before)).astype(jnp.float32)
        before = before + take * got
        group = jnp.where(earlier, group + same * got, got + same * group)
        step *= 2
    return before


def taylor_map(values):
    size = values.shape[-1]
    ones = jnp.ones(values.shape[:-1] + (1,), jnp.float32)
    pairs = (values[..., :, None] * values[..., None, :]).reshape(
        values.shape[:-1] + (size * size,)
    )
    return jnp.concatenate([ones, values, pairs * 0.5**0.5], axis=-1)


def segment_ids(positions, ends):
    return jnp.sum((positions[:, None] >= ends[None, :]).astype(jnp.int32), axis=1)


def local(tokens, w_in, conv_w, head_gain, w_out, prompt_lens, req_group, row_request):
    tok_rows = tokens.shape[0]
    width = 2 * FEAT + 2 * HD
    local_heads = w_in.shape[1] // width
    local_cols = local_heads * HD
    seq_pos = lax.axis_index("seq")
    first_row = seq_pos * tok_rows
    ends = jnp.cumsum(prompt_lens)
    starts = ends - prompt_lens
    positions = first_row + jnp.arange(tok_rows, dtype=jnp.int32)
    seg = segment_ids(positions, ends)
    proj = jnp.dot(
        lax.all_gather(tokens, "tp", axis=1, tiled=True), w_in, preferred_element_type=jnp.float32
    )
    proj = proj.astype(jnp.bfloat16).reshape(tok_rows, local_heads, width)
    gate_pre = proj[:, :, 2 * FEAT + HD :].reshape(tok_rows, local_cols)
    rim = passed_along(gate_pre[tok_rows - (KW - 1) :], "seq", 1)
    extended = jnp.concatenate([rim, gate_pre], 0)
    ext_pos = first_row - (KW - 1) + jnp.arange(tok_rows + KW - 1, dtype=jnp.int32)
    ext_seg = segment_ids(ext_pos, ends)
    gate = jnp.zeros((tok_rows, local_cols), jnp.float32)
    for tap in range(KW):
        low = KW - 1 - tap
        same = (ext_seg[low : low + tok_rows] == seg).astype(jnp.float32)
        gate = (
            gate
            + conv_w[tap][None, :]
            * extended[low : low + tok_rows].astype(jnp.float32)
            * same[:, None]
        )
    qs_b = proj[:, :, :FEAT] * jnp.bfloat16(FEAT ** (-0.25))
    ks_b = proj[:, :, FEAT : 2 * FEAT] * jnp.bfloat16(FEAT ** (-0.25))
    qs = qs_b.astype(jnp.float32)
    ks = ks_b.astype(jnp.float32)
    values = proj[:, :, 2 * FEAT : 2 * FEAT + HD]
    values_f = values.astype(jnp.float32)
    dots = jnp.einsum("thf,shf->hts", qs_b, ks_b, preferred_element_type=jnp.float32)
    visible = (positions[None, :] <= positions[:, None]) & (seg[:, None] == seg[None, :])
    weights = jnp.where(visible[None], 1.0 + dots + 0.5 * dots * dots, 0.0)
    numer = jnp.einsum(
        "hts,shd->thd", weights.astype(jnp.bfloat16), values, preferred_element_type=jnp.float32
    )
    phi_q = taylor_map(qs)
    phi_k = taylor_map(ks)
    fmap = phi_k.shape[-1]
    prompt_index = jnp.arange(PROMPTS, dtype=jnp.int32)
    onehot = (seg[:, None] == prompt_index[None, :]).astype(jnp.float32)
    keyed = (onehot[:, :, None, None] * phi_k[:, None, :, :]).reshape(
        tok_rows, PROMPTS * local_heads * fmap
    )
    contrib_state = lax.dot_general(
        keyed.reshape(tok_rows, PROMPTS, local_heads, fmap),
        values_f,
        (((0,), (0,)), ((2,), (1,))),
        precision=HIGH,
    )
    contrib_norm = jnp.einsum("tg,thf->ghf", onehot, phi_k, precision=HIGH)
    offsets = jnp.arange(KW - 1, dtype=jnp.int32)
    edge_rows = ends[:, None] - (KW - 1) + offsets[None, :]
    edge_valid = edge_rows >= starts[:, None]
    match = ((positions[:, None, None] == edge_rows[None]) & edge_valid[None]).astype(jnp.bfloat16)
    contrib_edge = jnp.einsum("tgj,tc->gjc", match, gate_pre, preferred_element_type=jnp.float32)
    block_ends = (jnp.arange(lax.axis_size("seq"), dtype=jnp.int32) + 1) * tok_rows - 1
    tail_seg = segment_ids(block_ends, ends)
    seg_last = tail_seg[seq_pos]
    tail_state = lax.dynamic_index_in_dim(contrib_state, seg_last, axis=1, keepdims=False)
    seg_before = jnp.sum((first_row - 1 >= ends).astype(jnp.int32))
    tails = lax.all_gather(tail_state.astype(jnp.bfloat16), "seq").astype(jnp.float32)
    block_index = jnp.arange(lax.axis_size("seq"), dtype=jnp.int32)
    chained = ((block_index < seq_pos) & (tail_seg == seg_before)).astype(jnp.float32)
    carry_state = jnp.sum(chained.reshape((-1,) + (1,) * (tails.ndim - 1)) * tails, axis=0)
    carried = ((seg == seg_before) & (first_row > 0)).astype(jnp.float32)
    attended = (
        numer
        + jnp.einsum("thf,hfd->thd", phi_q, carry_state, precision=HIGH) * carried[:, None, None]
    )
    inv_rms = lax.rsqrt(jnp.mean(attended * attended, axis=2, keepdims=True) + EPS)
    gain = head_gain.reshape(local_heads, HD)
    hidden = (
        attended * inv_rms * gain[None] * jax.nn.silu(gate.reshape(tok_rows, local_heads, HD))
    ).astype(jnp.bfloat16)
    hidden = hidden.reshape(tok_rows, local_cols)
    product = jnp.einsum(
        "tk,kgc->gtc",
        hidden,
        w_out.reshape(local_cols, lax.axis_size("tp"), -1),
        preferred_element_type=jnp.float32,
    )
    summed = lax.psum_scatter(
        lax.optimization_barrier(product.astype(jnp.bfloat16))
        .astype(jnp.float32)
        .astype(jnp.bfloat16),
        "tp",
        scatter_dimension=0,
        tiled=True,
    )
    mixed = summed.reshape(tok_rows, -1)
    all_state, all_norm, all_edge = psum_doubling((contrib_state, contrib_norm, contrib_edge), "seq")
    scale = lax.rsqrt(prompt_lens.astype(jnp.float32))
    my_requests = lax.dynamic_slice_in_dim(row_request, seq_pos * SLOTS, SLOTS)
    my_groups = jnp.take(req_group, my_requests)
    my_scale = jnp.take(scale, my_groups)
    req_state = jnp.take(all_state, my_groups, axis=1).transpose(1, 0, 2, 3) * my_scale[
        :, None, None, None
    ]
    req_norm = jnp.take(all_norm, my_groups, axis=0) * my_scale[:, None, None]
    req_edge = jnp.take(all_edge, my_groups, axis=0).astype(jnp.bfloat16)
    return (mixed, req_state, req_norm, req_edge)


def solution(mesh):
    in_specs = (
        P(("req", "seq"), "tp"),
        P(None, "tp"),
        P(None, "tp"),
        P("tp"),
        P("tp", None),
        P("req"),
        P("req"),
        P("req"),
    )
    out_specs = (
        P(("req", "seq"), "tp"),
        P(("req", "seq"), "tp", None, None),
        P(("req", "seq"), "tp", None),
        P(("req", "seq"), None, "tp"),
    )
    return jax.shard_map(local, mesh=mesh, in_specs=in_specs, out_specs=out_specs, check_vma=False)
```

```python
import jax
import jax.numpy as jnp
from jax import lax
from jax.sharding import PartitionSpec as P

FEAT = 16
HD = 112
KW = 3
PROMPTS = 4
SLOTS = 4


EPS = 1e-05
HIGH = lax.Precision.HIGHEST


def passed_along(shard, axis, by):
    size = lax.axis_size(axis)
    pairs = [(i, i + by) for i in range(size) if 0 <= i + by < size]
    return lax.ppermute(shard, axis, pairs)


def psum_doubling(parts, axis):
    size = lax.axis_size(axis)
    total = [p.astype(jnp.float32) for p in parts]
    step = 1
    while step < size:
        pairs = [(i, i ^ step) for i in range(size)]
        got = lax.ppermute(tuple(t.astype(jnp.bfloat16) for t in total), axis, pairs)
        total = [t + g.astype(jnp.float32) for t, g in zip(total, got)]
        step *= 2
    return total


def tail_prefix(tail, tail_seg, axis):
    size, here = (lax.axis_size(axis), lax.axis_index(axis))
    seg_before = tail_seg[jnp.maximum(here - 1, 0)]
    group = tail.astype(jnp.float32)
    before = jnp.zeros_like(group)
    step = 1
    while step < size:
        pairs = [(i, i ^ step) for i in range(size)]
        got = lax.ppermute(group.astype(jnp.bfloat16), axis, pairs).astype(jnp.float32)
        other = here ^ step
        my_end = (here | (step - 1))
        other_end = (other | (step - 1))
        same = (tail_seg[my_end] == tail_seg[other_end]).astype(jnp.float32)
        earlier = other < here
        take = (earlier & (tail_seg[other_end] == seg_before)).astype(jnp.float32)
        before = before + take * got
        group = jnp.where(earlier, group + same * got, got + same * group)
        step *= 2
    return before


def taylor_map(values):
    size = values.shape[-1]
    ones = jnp.ones(values.shape[:-1] + (1,), jnp.float32)
    pairs = (values[..., :, None] * values[..., None, :]).reshape(
        values.shape[:-1] + (size * size,)
    )
    return jnp.concatenate([ones, values, pairs * 0.5**0.5], axis=-1)


def segment_ids(positions, ends):
    return jnp.sum((positions[:, None] >= ends[None, :]).astype(jnp.int32), axis=1)


def local(tokens, w_in, conv_w, head_gain, w_out, prompt_lens, req_group, row_request):
    tok_rows = tokens.shape[0]
    width = 2 * FEAT + 2 * HD
    local_heads = w_in.shape[1] // width
    local_cols = local_heads * HD
    seq_pos = lax.axis_index("seq")
    first_row = seq_pos * tok_rows
    ends = jnp.cumsum(prompt_lens)
    starts = ends - prompt_lens
    positions = first_row + jnp.arange(tok_rows, dtype=jnp.int32)
    seg = segment_ids(positions, ends)
    proj = jnp.dot(
        lax.all_gather(tokens, "tp", axis=1, tiled=True), w_in, preferred_element_type=jnp.float32
    )
    proj = proj.astype(jnp.bfloat16).reshape(tok_rows, local_heads, width)
    gate_pre = proj[:, :, 2 * FEAT + HD :].reshape(tok_rows, local_cols)
    rim = passed_along(gate_pre[tok_rows - (KW - 1) :], "seq", 1)
    extended = jnp.concatenate([rim, gate_pre], 0)
    ext_pos = first_row - (KW - 1) + jnp.arange(tok_rows + KW - 1, dtype=jnp.int32)
    ext_seg = segment_ids(ext_pos, ends)
    gate = jnp.zeros((tok_rows, local_cols), jnp.float32)
    for tap in range(KW):
        low = KW - 1 - tap
        same = (ext_seg[low : low + tok_rows] == seg).astype(jnp.float32)
        gate = (
            gate
            + conv_w[tap][None, :]
            * extended[low : low + tok_rows].astype(jnp.float32)
            * same[:, None]
        )
    qs_b = proj[:, :, :FEAT] * jnp.bfloat16(FEAT ** (-0.25))
    ks_b = proj[:, :, FEAT : 2 * FEAT] * jnp.bfloat16(FEAT ** (-0.25))
    qs = qs_b.astype(jnp.float32)
    ks = ks_b.astype(jnp.float32)
    values = proj[:, :, 2 * FEAT : 2 * FEAT + HD]
    values_f = values.astype(jnp.float32)
    dots = jnp.einsum("thf,shf->hts", qs_b, ks_b, preferred_element_type=jnp.float32)
    visible = (positions[None, :] <= positions[:, None]) & (seg[:, None] == seg[None, :])
    weights = jnp.where(visible[None], 1.0 + dots + 0.5 * dots * dots, 0.0)
    numer = jnp.einsum(
        "hts,shd->thd", weights.astype(jnp.bfloat16), values, preferred_element_type=jnp.float32
    )
    phi_q = taylor_map(qs)
    phi_k = taylor_map(ks)
    fmap = phi_k.shape[-1]
    prompt_index = jnp.arange(PROMPTS, dtype=jnp.int32)
    onehot = (seg[:, None] == prompt_index[None, :]).astype(jnp.float32)
    keyed = (onehot[:, :, None, None] * phi_k[:, None, :, :]).reshape(
        tok_rows, PROMPTS * local_heads * fmap
    )
    contrib_state = lax.dot_general(
        keyed.reshape(tok_rows, PROMPTS, local_heads, fmap),
        values_f,
        (((0,), (0,)), ((2,), (1,))),
        precision=HIGH,
    )
    contrib_norm = jnp.einsum("tg,thf->ghf", onehot, phi_k, precision=HIGH)
    offsets = jnp.arange(KW - 1, dtype=jnp.int32)
    edge_rows = ends[:, None] - (KW - 1) + offsets[None, :]
    edge_valid = edge_rows >= starts[:, None]
    match = ((positions[:, None, None] == edge_rows[None]) & edge_valid[None]).astype(jnp.bfloat16)
    contrib_edge = jnp.einsum("tgj,tc->gjc", match, gate_pre, preferred_element_type=jnp.float32)
    block_ends = (jnp.arange(lax.axis_size("seq"), dtype=jnp.int32) + 1) * tok_rows - 1
    tail_seg = segment_ids(block_ends, ends)
    seg_last = tail_seg[seq_pos]
    in_tail = (seg == seg_last).astype(jnp.float32)
    tail_state = jnp.einsum(
        "thf,thd->hfd", phi_k * in_tail[:, None, None], values_f, precision=HIGH
    )
    seg_before = jnp.sum((first_row - 1 >= ends).astype(jnp.int32))
    tails = lax.all_gather(tail_state.astype(jnp.bfloat16), "seq").astype(jnp.float32)
    block_index = jnp.arange(lax.axis_size("seq"), dtype=jnp.int32)
    chained = ((block_index < seq_pos) & (tail_seg == seg_before)).astype(jnp.float32)
    carry_state = jnp.sum(chained.reshape((-1,) + (1,) * (tails.ndim - 1)) * tails, axis=0)
    carried = ((seg == seg_before) & (first_row > 0)).astype(jnp.float32)
    attended = (
        numer
        + jnp.einsum("thf,hfd->thd", phi_q, carry_state, precision=HIGH) * carried[:, None, None]
    )
    inv_rms = lax.rsqrt(jnp.mean(attended * attended, axis=2, keepdims=True) + EPS)
    gain = head_gain.reshape(local_heads, HD)
    hidden = (
        attended * inv_rms * gain[None] * jax.nn.silu(gate.reshape(tok_rows, local_heads, HD))
    ).astype(jnp.bfloat16)
    hidden = hidden.reshape(tok_rows, local_cols)
    product = jnp.einsum(
        "tk,kgc->gtc",
        hidden,
        w_out.reshape(local_cols, lax.axis_size("tp"), -1),
        preferred_element_type=jnp.bfloat16,
    )
    summed = lax.psum_scatter(
        product,
        "tp",
        scatter_dimension=0,
        tiled=True,
    )
    mixed = summed.reshape(tok_rows, -1)
    all_state, all_norm, all_edge = psum_doubling((contrib_state, contrib_norm, contrib_edge), "seq")
    scale = lax.rsqrt(prompt_lens.astype(jnp.float32))
    my_requests = lax.dynamic_slice_in_dim(row_request, seq_pos * SLOTS, SLOTS)
    my_groups = jnp.take(req_group, my_requests)
    my_scale = jnp.take(scale, my_groups)
    req_state = jnp.take(all_state, my_groups, axis=1).transpose(1, 0, 2, 3) * my_scale[
        :, None, None, None
    ]
    req_norm = jnp.take(all_norm, my_groups, axis=0) * my_scale[:, None, None]
    req_edge = jnp.take(all_edge, my_groups, axis=0).astype(jnp.bfloat16)
    return (mixed, req_state, req_norm, req_edge)


def solution(mesh):
    in_specs = (
        P(("req", "seq"), "tp"),
        P(None, "tp"),
        P(None, "tp"),
        P("tp"),
        P("tp", None),
        P("req"),
        P("req"),
        P("req"),
    )
    out_specs = (
        P(("req", "seq"), "tp"),
        P(("req", "seq"), "tp", None, None),
        P(("req", "seq"), "tp", None),
        P(("req", "seq"), None, "tp"),
    )
    return jax.shard_map(local, mesh=mesh, in_specs=in_specs, out_specs=out_specs, check_vma=False)
```

```python
import jax
import jax.numpy as jnp
from jax import lax
from jax.sharding import PartitionSpec as P

FEAT = 16
HD = 112
KW = 3
PROMPTS = 4
SLOTS = 4


EPS = 1e-05
HIGH = lax.Precision.HIGHEST


def passed_along(shard, axis, by):
    size = lax.axis_size(axis)
    pairs = [(i, i + by) for i in range(size) if 0 <= i + by < size]
    return lax.ppermute(shard, axis, pairs)


def psum_doubling(parts, axis):
    size = lax.axis_size(axis)
    total = [p.astype(jnp.float32) for p in parts]
    step = 1
    while step < size:
        pairs = [(i, i ^ step) for i in range(size)]
        got = lax.ppermute(tuple(t.astype(jnp.bfloat16) for t in total), axis, pairs)
        total = [t + g.astype(jnp.float32) for t, g in zip(total, got)]
        step *= 2
    return total


def tail_prefix(tail, tail_seg, axis):
    size, here = (lax.axis_size(axis), lax.axis_index(axis))
    seg_before = tail_seg[jnp.maximum(here - 1, 0)]
    group = tail.astype(jnp.float32)
    before = jnp.zeros_like(group)
    step = 1
    while step < size:
        pairs = [(i, i ^ step) for i in range(size)]
        got = lax.ppermute(group.astype(jnp.bfloat16), axis, pairs).astype(jnp.float32)
        other = here ^ step
        my_end = (here | (step - 1))
        other_end = (other | (step - 1))
        same = (tail_seg[my_end] == tail_seg[other_end]).astype(jnp.float32)
        earlier = other < here
        take = (earlier & (tail_seg[other_end] == seg_before)).astype(jnp.float32)
        before = before + take * got
        group = jnp.where(earlier, group + same * got, got + same * group)
        step *= 2
    return before


def taylor_map(values):
    size = values.shape[-1]
    ones = jnp.ones(values.shape[:-1] + (1,), jnp.float32)
    pairs = (values[..., :, None] * values[..., None, :]).reshape(
        values.shape[:-1] + (size * size,)
    )
    return jnp.concatenate([ones, values, pairs * 0.5**0.5], axis=-1)


def segment_ids(positions, ends):
    return jnp.sum((positions[:, None] >= ends[None, :]).astype(jnp.int32), axis=1)


def local(tokens, w_in, conv_w, head_gain, w_out, prompt_lens, req_group, row_request):
    tok_rows = tokens.shape[0]
    width = 2 * FEAT + 2 * HD
    local_heads = w_in.shape[1] // width
    local_cols = local_heads * HD
    seq_pos = lax.axis_index("seq")
    first_row = seq_pos * tok_rows
    ends = jnp.cumsum(prompt_lens)
    starts = ends - prompt_lens
    positions = first_row + jnp.arange(tok_rows, dtype=jnp.int32)
    seg = segment_ids(positions, ends)
    half = tok_rows // 2
    proj_halves = [
        jnp.dot(
            lax.all_gather(part, "tp", axis=1, tiled=True), w_in, preferred_element_type=jnp.float32
        )
        .astype(jnp.bfloat16)
        .reshape(half, local_heads, width)
        for part in (tokens[:half], tokens[half:])
    ]
    proj = jnp.concatenate(proj_halves, axis=0)
    gate_pre = proj[:, :, 2 * FEAT + HD :].reshape(tok_rows, local_cols)
    rim = passed_along(gate_pre[tok_rows - (KW - 1) :], "seq", 1)
    extended = jnp.concatenate([rim, gate_pre], 0)
    ext_pos = first_row - (KW - 1) + jnp.arange(tok_rows + KW - 1, dtype=jnp.int32)
    ext_seg = segment_ids(ext_pos, ends)
    gate = jnp.zeros((tok_rows, local_cols), jnp.float32)
    for tap in range(KW):
        low = KW - 1 - tap
        same = (ext_seg[low : low + tok_rows] == seg).astype(jnp.float32)
        gate = (
            gate
            + conv_w[tap][None, :]
            * extended[low : low + tok_rows].astype(jnp.float32)
            * same[:, None]
        )
    qs_b = proj[:, :, :FEAT] * jnp.bfloat16(FEAT ** (-0.25))
    ks_b = proj[:, :, FEAT : 2 * FEAT] * jnp.bfloat16(FEAT ** (-0.25))
    qs = qs_b.astype(jnp.float32)
    ks = ks_b.astype(jnp.float32)
    values = proj[:, :, 2 * FEAT : 2 * FEAT + HD]
    values_f = values.astype(jnp.float32)
    numer_halves = []
    for lo, hi in ((0, half), (half, tok_rows)):
        dots = jnp.einsum(
            "thf,shf->hts", qs_b[lo:hi], ks_b[:hi], preferred_element_type=jnp.float32
        )
        visible = (positions[None, :hi] <= positions[lo:hi, None]) & (
            seg[lo:hi, None] == seg[None, :hi]
        )
        weights = jnp.where(visible[None], 1.0 + dots + 0.5 * dots * dots, 0.0)
        numer_halves.append(
            jnp.einsum(
                "hts,shd->thd",
                weights.astype(jnp.bfloat16),
                values[:hi],
                preferred_element_type=jnp.float32,
            )
        )
    numer = jnp.concatenate(numer_halves, axis=0)
    phi_q = taylor_map(qs)
    phi_k = taylor_map(ks)
    fmap = phi_k.shape[-1]
    prompt_index = jnp.arange(PROMPTS, dtype=jnp.int32)
    onehot = (seg[:, None] == prompt_index[None, :]).astype(jnp.float32)
    keyed = (onehot[:, :, None, None] * phi_k[:, None, :, :]).reshape(
        tok_rows, PROMPTS * local_heads * fmap
    )
    contrib_state = lax.dot_general(
        keyed.reshape(tok_rows, PROMPTS, local_heads, fmap),
        values_f,
        (((0,), (0,)), ((2,), (1,))),
        precision=HIGH,
    )
    contrib_norm = jnp.einsum("tg,thf->ghf", onehot, phi_k, precision=HIGH)
    offsets = jnp.arange(KW - 1, dtype=jnp.int32)
    edge_rows = ends[:, None] - (KW - 1) + offsets[None, :]
    edge_valid = edge_rows >= starts[:, None]
    match = ((positions[:, None, None] == edge_rows[None]) & edge_valid[None]).astype(jnp.bfloat16)
    contrib_edge = jnp.einsum("tgj,tc->gjc", match, gate_pre, preferred_element_type=jnp.float32)
    block_ends = (jnp.arange(lax.axis_size("seq"), dtype=jnp.int32) + 1) * tok_rows - 1
    tail_seg = segment_ids(block_ends, ends)
    seg_last = tail_seg[seq_pos]
    in_tail = (seg == seg_last).astype(jnp.float32)
    tail_state = sum(
        jnp.einsum(
            "thf,thd->hfd",
            taylor_map(ks[lo:hi]) * in_tail[lo:hi, None, None],
            values_f[lo:hi],
            precision=HIGH,
        )
        for lo, hi in ((0, half), (half, tok_rows))
    )
    seg_before = jnp.sum((first_row - 1 >= ends).astype(jnp.int32))
    tails = lax.all_gather(tail_state.astype(jnp.bfloat16), "seq").astype(jnp.float32)
    block_index = jnp.arange(lax.axis_size("seq"), dtype=jnp.int32)
    chained = ((block_index < seq_pos) & (tail_seg == seg_before)).astype(jnp.float32)
    carry_state = jnp.sum(chained.reshape((-1,) + (1,) * (tails.ndim - 1)) * tails, axis=0)
    carried = ((seg == seg_before) & (first_row > 0)).astype(jnp.float32)
    attended = (
        numer
        + jnp.einsum("thf,hfd->thd", phi_q, carry_state, precision=HIGH) * carried[:, None, None]
    )
    inv_rms = lax.rsqrt(jnp.mean(attended * attended, axis=2, keepdims=True) + EPS)
    gain = head_gain.reshape(local_heads, HD)
    hidden = (
        attended * inv_rms * gain[None] * jax.nn.silu(gate.reshape(tok_rows, local_heads, HD))
    ).astype(jnp.bfloat16)
    hidden = hidden.reshape(tok_rows, local_cols)
    product = jnp.einsum(
        "tk,kgc->gtc",
        hidden,
        w_out.reshape(local_cols, lax.axis_size("tp"), -1),
        preferred_element_type=jnp.bfloat16,
    )
    summed = lax.psum_scatter(
        product,
        "tp",
        scatter_dimension=0,
        tiled=True,
    )
    mixed = summed.reshape(tok_rows, -1)
    all_state, all_norm, all_edge = psum_doubling((contrib_state, contrib_norm, contrib_edge), "seq")
    scale = lax.rsqrt(prompt_lens.astype(jnp.float32))
    my_requests = lax.dynamic_slice_in_dim(row_request, seq_pos * SLOTS, SLOTS)
    my_groups = jnp.take(req_group, my_requests)
    my_scale = jnp.take(scale, my_groups)
    req_state = jnp.take(all_state, my_groups, axis=1).transpose(1, 0, 2, 3) * my_scale[
        :, None, None, None
    ]
    req_norm = jnp.take(all_norm, my_groups, axis=0) * my_scale[:, None, None]
    req_edge = jnp.take(all_edge, my_groups, axis=0).astype(jnp.bfloat16)
    return (mixed, req_state, req_norm, req_edge)


def solution(mesh):
    in_specs = (
        P(("req", "seq"), "tp"),
        P(None, "tp"),
        P(None, "tp"),
        P("tp"),
        P("tp", None),
        P("req"),
        P("req"),
        P("req"),
    )
    out_specs = (
        P(("req", "seq"), "tp"),
        P(("req", "seq"), "tp", None, None),
        P(("req", "seq"), "tp", None),
        P(("req", "seq"), None, "tp"),
    )
    return jax.shard_map(local, mesh=mesh, in_specs=in_specs, out_specs=out_specs, check_vma=False)
```

```python
import jax
import jax.numpy as jnp
from jax import lax
from jax.sharding import PartitionSpec as P

FEAT = 16
HD = 112
KW = 3
PROMPTS = 4
SLOTS = 4


EPS = 1e-05
HIGH = lax.Precision.HIGHEST


def passed_along(shard, axis, by):
    size = lax.axis_size(axis)
    pairs = [(i, i + by) for i in range(size) if 0 <= i + by < size]
    return lax.ppermute(shard, axis, pairs)


def psum_doubling(parts, axis):
    size = lax.axis_size(axis)
    total = [p.astype(jnp.float32) for p in parts]
    step = 1
    while step < size:
        pairs = [(i, i ^ step) for i in range(size)]
        got = lax.ppermute(tuple(t.astype(jnp.bfloat16) for t in total), axis, pairs)
        total = [t + g.astype(jnp.float32) for t, g in zip(total, got)]
        step *= 2
    return total


def tail_prefix(tail, tail_seg, axis):
    size, here = (lax.axis_size(axis), lax.axis_index(axis))
    seg_before = tail_seg[jnp.maximum(here - 1, 0)]
    group = tail.astype(jnp.float32)
    before = jnp.zeros_like(group)
    step = 1
    while step < size:
        pairs = [(i, i ^ step) for i in range(size)]
        got = lax.ppermute(group.astype(jnp.bfloat16), axis, pairs).astype(jnp.float32)
        other = here ^ step
        my_end = (here | (step - 1))
        other_end = (other | (step - 1))
        same = (tail_seg[my_end] == tail_seg[other_end]).astype(jnp.float32)
        earlier = other < here
        take = (earlier & (tail_seg[other_end] == seg_before)).astype(jnp.float32)
        before = before + take * got
        group = jnp.where(earlier, group + same * got, got + same * group)
        step *= 2
    return before


def taylor_map(values):
    size = values.shape[-1]
    ones = jnp.ones(values.shape[:-1] + (1,), jnp.float32)
    pairs = (values[..., :, None] * values[..., None, :]).reshape(
        values.shape[:-1] + (size * size,)
    )
    return jnp.concatenate([ones, values, pairs * 0.5**0.5], axis=-1)


def segment_ids(positions, ends):
    return jnp.sum((positions[:, None] >= ends[None, :]).astype(jnp.int32), axis=1)


def local(tokens, w_in, conv_w, head_gain, w_out, prompt_lens, req_group, row_request):
    tok_rows = tokens.shape[0]
    width = 2 * FEAT + 2 * HD
    local_heads = w_in.shape[1] // width
    local_cols = local_heads * HD
    seq_pos = lax.axis_index("seq")
    first_row = seq_pos * tok_rows
    ends = jnp.cumsum(prompt_lens)
    starts = ends - prompt_lens
    positions = first_row + jnp.arange(tok_rows, dtype=jnp.int32)
    seg = segment_ids(positions, ends)
    proj = jnp.dot(
        lax.all_gather(tokens, "tp", axis=1, tiled=True), w_in, preferred_element_type=jnp.float32
    )
    proj = proj.astype(jnp.bfloat16).reshape(tok_rows, local_heads, width)
    gate_pre = proj[:, :, 2 * FEAT + HD :].reshape(tok_rows, local_cols)
    rim = passed_along(gate_pre[tok_rows - (KW - 1) :], "seq", 1)
    extended = jnp.concatenate([rim, gate_pre], 0)
    ext_pos = first_row - (KW - 1) + jnp.arange(tok_rows + KW - 1, dtype=jnp.int32)
    ext_seg = segment_ids(ext_pos, ends)
    gate = jnp.zeros((tok_rows, local_cols), jnp.float32)
    for tap in range(KW):
        low = KW - 1 - tap
        same = (ext_seg[low : low + tok_rows] == seg).astype(jnp.float32)
        gate = (
            gate
            + conv_w[tap][None, :]
            * extended[low : low + tok_rows].astype(jnp.float32)
            * same[:, None]
        )
    qs_b = proj[:, :, :FEAT] * jnp.bfloat16(FEAT ** (-0.25))
    ks_b = proj[:, :, FEAT : 2 * FEAT] * jnp.bfloat16(FEAT ** (-0.25))
    qs = qs_b.astype(jnp.float32)
    ks = ks_b.astype(jnp.float32)
    values = proj[:, :, 2 * FEAT : 2 * FEAT + HD]
    values_f = values.astype(jnp.float32)
    dots = jnp.einsum("thf,shf->hts", qs_b, ks_b, preferred_element_type=jnp.float32)
    visible = (positions[None, :] <= positions[:, None]) & (seg[:, None] == seg[None, :])
    weights = jnp.where(visible[None], 1.0 + dots + 0.5 * dots * dots, 0.0)
    numer = jnp.einsum(
        "hts,shd->thd", weights.astype(jnp.bfloat16), values, preferred_element_type=jnp.float32
    )
    phi_q = taylor_map(qs)
    phi_k = taylor_map(ks)
    fmap = phi_k.shape[-1]
    prompt_index = jnp.arange(PROMPTS, dtype=jnp.int32)
    onehot = (seg[:, None] == prompt_index[None, :]).astype(jnp.float32)
    keyed = (onehot[:, :, None, None] * phi_k[:, None, :, :]).reshape(
        tok_rows, PROMPTS * local_heads * fmap
    )
    contrib_state = lax.dot_general(
        keyed.reshape(tok_rows, PROMPTS, local_heads, fmap),
        values_f,
        (((0,), (0,)), ((2,), (1,))),
        precision=HIGH,
    )
    contrib_norm = jnp.einsum("tg,thf->ghf", onehot, phi_k, precision=HIGH)
    offsets = jnp.arange(KW - 1, dtype=jnp.int32)
    edge_rows = ends[:, None] - (KW - 1) + offsets[None, :]
    edge_valid = edge_rows >= starts[:, None]
    match = ((positions[:, None, None] == edge_rows[None]) & edge_valid[None]).astype(jnp.bfloat16)
    contrib_edge = jnp.einsum("tgj,tc->gjc", match, gate_pre, preferred_element_type=jnp.float32)
    block_ends = (jnp.arange(lax.axis_size("seq"), dtype=jnp.int32) + 1) * tok_rows - 1
    tail_seg = segment_ids(block_ends, ends)
    seg_last = tail_seg[seq_pos]
    in_tail = (seg == seg_last).astype(jnp.float32)
    tail_state = jnp.einsum(
        "thf,thd->hfd", phi_k * in_tail[:, None, None], values_f, precision=HIGH
    )
    seg_before = jnp.sum((first_row - 1 >= ends).astype(jnp.int32))
    tails = lax.all_gather(tail_state.astype(jnp.bfloat16), "seq").astype(jnp.float32)
    block_index = jnp.arange(lax.axis_size("seq"), dtype=jnp.int32)
    chained = ((block_index < seq_pos) & (tail_seg == seg_before)).astype(jnp.float32)
    carry_state = jnp.sum(chained.reshape((-1,) + (1,) * (tails.ndim - 1)) * tails, axis=0)
    carried = ((seg == seg_before) & (first_row > 0)).astype(jnp.float32)
    attended = (
        numer
        + jnp.einsum("thf,hfd->thd", phi_q, carry_state, precision=HIGH) * carried[:, None, None]
    )
    inv_rms = lax.rsqrt(jnp.mean(attended * attended, axis=2, keepdims=True) + EPS)
    gain = head_gain.reshape(local_heads, HD)
    hidden = (
        attended * inv_rms * gain[None] * jax.nn.silu(gate.reshape(tok_rows, local_heads, HD))
    ).astype(jnp.bfloat16)
    hidden = hidden.reshape(tok_rows, local_cols)
    n_tp = lax.axis_size("tp")
    w_cols = lax.all_to_all(
        w_out.reshape(local_cols, n_tp, -1), "tp", split_axis=1, concat_axis=0, tiled=True
    ).reshape(n_tp, local_cols, -1)
    hidden_all = lax.all_gather(hidden, "tp", axis=1, tiled=True).reshape(tok_rows, n_tp, local_cols)
    partial = jnp.einsum(
        "tgk,gkc->gtc", hidden_all, w_cols, preferred_element_type=jnp.bfloat16
    )
    mixed = jnp.sum(partial.astype(jnp.float32), axis=0).astype(jnp.bfloat16)
    all_state, all_norm, all_edge = psum_doubling((contrib_state, contrib_norm, contrib_edge), "seq")
    scale = lax.rsqrt(prompt_lens.astype(jnp.float32))
    my_requests = lax.dynamic_slice_in_dim(row_request, seq_pos * SLOTS, SLOTS)
    my_groups = jnp.take(req_group, my_requests)
    my_scale = jnp.take(scale, my_groups)
    req_state = jnp.take(all_state, my_groups, axis=1).transpose(1, 0, 2, 3) * my_scale[
        :, None, None, None
    ]
    req_norm = jnp.take(all_norm, my_groups, axis=0) * my_scale[:, None, None]
    req_edge = jnp.take(all_edge, my_groups, axis=0).astype(jnp.bfloat16)
    return (mixed, req_state, req_norm, req_edge)


def solution(mesh):
    in_specs = (
        P(("req", "seq"), "tp"),
        P(None, "tp"),
        P(None, "tp"),
        P("tp"),
        P("tp", None),
        P("req"),
        P("req"),
        P("req"),
    )
    out_specs = (
        P(("req", "seq"), "tp"),
        P(("req", "seq"), "tp", None, None),
        P(("req", "seq"), "tp", None),
        P(("req", "seq"), None, "tp"),
    )
    return jax.shard_map(local, mesh=mesh, in_specs=in_specs, out_specs=out_specs, check_vma=False)
```

```python
import jax
import jax.numpy as jnp
from jax import lax
from jax.sharding import PartitionSpec as P

FEAT = 16
HD = 112
KW = 3
PROMPTS = 4
SLOTS = 4


EPS = 1e-05
HIGH = lax.Precision.HIGHEST


def passed_along(shard, axis, by):
    size = lax.axis_size(axis)
    pairs = [(i, i + by) for i in range(size) if 0 <= i + by < size]
    return lax.ppermute(shard, axis, pairs)


def psum_doubling(parts, axis):
    size = lax.axis_size(axis)
    total = [p.astype(jnp.float32) for p in parts]
    step = 1
    while step < size:
        pairs = [(i, i ^ step) for i in range(size)]
        got = lax.ppermute(tuple(t.astype(jnp.bfloat16) for t in total), axis, pairs)
        total = [t + g.astype(jnp.float32) for t, g in zip(total, got)]
        step *= 2
    return total


def tail_prefix(tail, tail_seg, axis):
    size, here = (lax.axis_size(axis), lax.axis_index(axis))
    seg_before = tail_seg[jnp.maximum(here - 1, 0)]
    group = tail.astype(jnp.float32)
    before = jnp.zeros_like(group)
    step = 1
    while step < size:
        pairs = [(i, i ^ step) for i in range(size)]
        got = lax.ppermute(group.astype(jnp.bfloat16), axis, pairs).astype(jnp.float32)
        other = here ^ step
        my_end = (here | (step - 1))
        other_end = (other | (step - 1))
        same = (tail_seg[my_end] == tail_seg[other_end]).astype(jnp.float32)
        earlier = other < here
        take = (earlier & (tail_seg[other_end] == seg_before)).astype(jnp.float32)
        before = before + take * got
        group = jnp.where(earlier, group + same * got, got + same * group)
        step *= 2
    return before


def taylor_map(values):
    size = values.shape[-1]
    ones = jnp.ones(values.shape[:-1] + (1,), jnp.float32)
    pairs = (values[..., :, None] * values[..., None, :]).reshape(
        values.shape[:-1] + (size * size,)
    )
    return jnp.concatenate([ones, values, pairs * 0.5**0.5], axis=-1)


def segment_ids(positions, ends):
    return jnp.sum((positions[:, None] >= ends[None, :]).astype(jnp.int32), axis=1)


def local(tokens, w_in, conv_w, head_gain, w_out, prompt_lens, req_group, row_request):
    tok_rows = tokens.shape[0]
    width = 2 * FEAT + 2 * HD
    local_heads = w_in.shape[1] // width
    local_cols = local_heads * HD
    seq_pos = lax.axis_index("seq")
    first_row = seq_pos * tok_rows
    ends = jnp.cumsum(prompt_lens)
    starts = ends - prompt_lens
    positions = first_row + jnp.arange(tok_rows, dtype=jnp.int32)
    seg = segment_ids(positions, ends)
    proj = jnp.dot(
        lax.all_gather(tokens, "tp", axis=1, tiled=True), w_in, preferred_element_type=jnp.float32
    )
    proj = proj.astype(jnp.bfloat16).reshape(tok_rows, local_heads, width)
    gate_pre = proj[:, :, 2 * FEAT + HD :].reshape(tok_rows, local_cols)
    own_rim = gate_pre[tok_rows - (KW - 1) :]
    qs_b = proj[:, :, :FEAT] * jnp.bfloat16(FEAT ** (-0.25))
    ks_b = proj[:, :, FEAT : 2 * FEAT] * jnp.bfloat16(FEAT ** (-0.25))
    qs = qs_b.astype(jnp.float32)
    ks = ks_b.astype(jnp.float32)
    values = proj[:, :, 2 * FEAT : 2 * FEAT + HD]
    values_f = values.astype(jnp.float32)
    dots = jnp.einsum("thf,shf->hts", qs_b, ks_b, preferred_element_type=jnp.float32)
    visible = (positions[None, :] <= positions[:, None]) & (seg[:, None] == seg[None, :])
    weights = jnp.where(visible[None], 1.0 + dots + 0.5 * dots * dots, 0.0)
    numer = jnp.einsum(
        "hts,shd->thd", weights.astype(jnp.bfloat16), values, preferred_element_type=jnp.float32
    )
    phi_q = taylor_map(qs)
    phi_k = taylor_map(ks)
    fmap = phi_k.shape[-1]
    prompt_index = jnp.arange(PROMPTS, dtype=jnp.int32)
    onehot = (seg[:, None] == prompt_index[None, :]).astype(jnp.float32)
    keyed = (onehot[:, :, None, None] * phi_k[:, None, :, :]).reshape(
        tok_rows, PROMPTS * local_heads * fmap
    )
    contrib_state = lax.dot_general(
        keyed.reshape(tok_rows, PROMPTS, local_heads, fmap),
        values_f,
        (((0,), (0,)), ((2,), (1,))),
        precision=HIGH,
    )
    contrib_norm = jnp.einsum("tg,thf->ghf", onehot, phi_k, precision=HIGH)
    offsets = jnp.arange(KW - 1, dtype=jnp.int32)
    edge_rows = ends[:, None] - (KW - 1) + offsets[None, :]
    edge_valid = edge_rows >= starts[:, None]
    match = ((positions[:, None, None] == edge_rows[None]) & edge_valid[None]).astype(jnp.bfloat16)
    contrib_edge = jnp.einsum("tgj,tc->gjc", match, gate_pre, preferred_element_type=jnp.float32)
    block_ends = (jnp.arange(lax.axis_size("seq"), dtype=jnp.int32) + 1) * tok_rows - 1
    tail_seg = segment_ids(block_ends, ends)
    seg_last = tail_seg[seq_pos]
    in_tail = (seg == seg_last).astype(jnp.float32)
    tail_state = jnp.einsum(
        "thf,thd->hfd", phi_k * in_tail[:, None, None], values_f, precision=HIGH
    )
    seg_before = jnp.sum((first_row - 1 >= ends).astype(jnp.int32))
    fmap_rows = tail_state.shape[1]
    shared = lax.all_gather(
        jnp.concatenate(
            [tail_state.astype(jnp.bfloat16), own_rim.reshape(1, KW - 1, -1)], axis=1
        ),
        "seq",
    )
    tails = shared[:, :, :fmap_rows].astype(jnp.float32)
    rim = lax.dynamic_index_in_dim(
        shared[:, 0, fmap_rows:], jnp.maximum(seq_pos - 1, 0), axis=0, keepdims=False
    ) * (seq_pos > 0).astype(jnp.bfloat16)
    extended = jnp.concatenate([rim, gate_pre], 0)
    ext_pos = first_row - (KW - 1) + jnp.arange(tok_rows + KW - 1, dtype=jnp.int32)
    ext_seg = segment_ids(ext_pos, ends)
    gate = jnp.zeros((tok_rows, local_cols), jnp.float32)
    for tap in range(KW):
        low = KW - 1 - tap
        same = (ext_seg[low : low + tok_rows] == seg).astype(jnp.float32)
        gate = (
            gate
            + conv_w[tap][None, :]
            * extended[low : low + tok_rows].astype(jnp.float32)
            * same[:, None]
        )
    block_index = jnp.arange(lax.axis_size("seq"), dtype=jnp.int32)
    chained = ((block_index < seq_pos) & (tail_seg == seg_before)).astype(jnp.float32)
    carry_state = jnp.sum(chained.reshape((-1,) + (1,) * (tails.ndim - 1)) * tails, axis=0)
    carried = ((seg == seg_before) & (first_row > 0)).astype(jnp.float32)
    attended = (
        numer
        + jnp.einsum("thf,hfd->thd", phi_q, carry_state, precision=HIGH) * carried[:, None, None]
    )
    inv_rms = lax.rsqrt(jnp.mean(attended * attended, axis=2, keepdims=True) + EPS)
    gain = head_gain.reshape(local_heads, HD)
    hidden = (
        attended * inv_rms * gain[None] * jax.nn.silu(gate.reshape(tok_rows, local_heads, HD))
    ).astype(jnp.bfloat16)
    hidden = hidden.reshape(tok_rows, local_cols)
    product = jnp.einsum(
        "tk,kgc->gtc",
        hidden,
        w_out.reshape(local_cols, lax.axis_size("tp"), -1),
        preferred_element_type=jnp.bfloat16,
    )
    summed = lax.psum_scatter(
        product,
        "tp",
        scatter_dimension=0,
        tiled=True,
    )
    mixed = summed.reshape(tok_rows, -1)
    all_state, all_norm, all_edge = psum_doubling((contrib_state, contrib_norm, contrib_edge), "seq")
    scale = lax.rsqrt(prompt_lens.astype(jnp.float32))
    my_requests = lax.dynamic_slice_in_dim(row_request, seq_pos * SLOTS, SLOTS)
    my_groups = jnp.take(req_group, my_requests)
    my_scale = jnp.take(scale, my_groups)
    req_state = jnp.take(all_state, my_groups, axis=1).transpose(1, 0, 2, 3) * my_scale[
        :, None, None, None
    ]
    req_norm = jnp.take(all_norm, my_groups, axis=0) * my_scale[:, None, None]
    req_edge = jnp.take(all_edge, my_groups, axis=0).astype(jnp.bfloat16)
    return (mixed, req_state, req_norm, req_edge)


def solution(mesh):
    in_specs = (
        P(("req", "seq"), "tp"),
        P(None, "tp"),
        P(None, "tp"),
        P("tp"),
        P("tp", None),
        P("req"),
        P("req"),
        P("req"),
    )
    out_specs = (
        P(("req", "seq"), "tp"),
        P(("req", "seq"), "tp", None, None),
        P(("req", "seq"), "tp", None),
        P(("req", "seq"), None, "tp"),
    )
    return jax.shard_map(local, mesh=mesh, in_specs=in_specs, out_specs=out_specs, check_vma=False)
```
